512 devices in a mesh: day: 64 (over x, z_lo, core), pair: 8 (over y, z_hi).
Axes of the slice: x: 4, y: 4, z: 16 (z_hi: 2, z_lo: 8; z = z_hi * 8 + z_lo), core: 2. Of those that a mesh axis runs over, the one named last changes fastest.
Arguments:
- spectra: bfloat16 [256, 128, 1024], P('day', 'pair'), may hold values from -4 to 4
- pair_list: int32 [4096, 2], P('pair'), may hold values from 0 to 127, as said below
- mask: int32 [256, 128], P('day'), may hold values from 0 to 1
Outputs:
- linear_stack: float32 [401, 4096], P(None, ('pair', 'day'))
- weighted_stack: float32 [401, 4096], P(None, ('pair', 'day'))
The draws below stay inside these ranges and needn't reach their ends.
Inputs may be any that keep to these rules, and one draw needn't show every extreme that they name: `pair_list`: the two stations of a pair differ.
All inputs are finite; a program needn't handle non-finite values.
Results may differ from the reference program's by a relative error of at most 0.0039.
Values may be sent and summed in bfloat16 or wider, within the bound.
No kernel may reach another device: no remote copies, remote signals or barrier semaphores. Data moves between devices by JAX's collectives and lax.ppermute only.
A program may use at most 64 MiB of HBM per device.

```python
import math
import jax
import jax.numpy as jnp
from jax import lax

F = 512
MAXLAG = 200
STATIONS = 128
LAGS = 401
DAYS = 256
PAIRS = 4096


def draw_spectra(key, part):
    first_key, second_key = jax.random.split(jax.random.fold_in(key, 11))
    common = jax.random.normal(first_key, (STATIONS, 2 * F), jnp.float32)
    noise = jax.random.normal(second_key, (DAYS, STATIONS, 2 * F), jnp.float32)
    whole = 0.8 * common[None] + 0.6 * noise
    return jnp.clip(whole, -4.0, 4.0).astype(jnp.bfloat16)


def draw_pair_list(key, part):
    first_key, second_key = jax.random.split(jax.random.fold_in(key, 23))
    first = jax.random.randint(first_key, (PAIRS,), 0, STATIONS, jnp.int32)
    offset = jax.random.randint(second_key, (PAIRS,), 1, STATIONS, jnp.int32)
    second = jnp.mod(first + offset, STATIONS)
    first = first.at[0].set(0)
    second = second.at[0].set(STATIONS - 1)
    return jnp.stack([first, second], 1).astype(jnp.int32)


def draw_mask(key, part):
    draws = jax.random.randint(jax.random.fold_in(key, 37), (DAYS, STATIONS), 0, 1000, jnp.int32)
    day_index = jnp.arange(DAYS, dtype=jnp.int32)
    limit = 300 + 600 * day_index // max(DAYS - 1, 1)
    live = (draws < limit[:, None]).astype(jnp.int32)
    return jnp.where(day_index[:, None] == 0, 1, live).astype(jnp.int32)


def setup_inputs(seed: int = 0) -> dict:
    splits = jax.random.split(jax.random.key(seed), 4)
    spectra = draw_spectra(jax.random.fold_in(splits[3], 71), 0)
    pair_list = draw_pair_list(jax.random.fold_in(splits[3], 71), 0)
    mask = draw_mask(jax.random.fold_in(splits[3], 71), 0)
    return dict(spectra=spectra, pair_list=pair_list, mask=mask)


def lag_table():
    lag = jnp.arange(LAGS, dtype=jnp.int32) - MAXLAG
    freq = jnp.arange(F, dtype=jnp.int32)
    phase = jnp.mod(lag[:, None] * freq[None, :], 2 * F).astype(jnp.float32) * (math.pi / F)
    scale = 1.0 / math.sqrt(F)
    cosine = jnp.cos(phase) * scale
    sine = jnp.sin(phase) * scale
    upper = jnp.concatenate([cosine, -sine], 1)
    lower = jnp.concatenate([sine, cosine], 1)
    return jnp.concatenate([upper, lower], 0).astype(jnp.bfloat16)

def reference(spectra, pair_list, mask):
    table = lag_table()
    first = pair_list[:, 0].astype(jnp.int32)
    second = pair_list[:, 1].astype(jnp.int32)
    mask_float = mask.astype(jnp.float32)
    weights = jnp.take(mask_float, first, axis=1) * jnp.take(mask_float, second, axis=1)

    def one_day(carry, inputs):
        day_spec, weight = inputs
        left = jnp.take(day_spec, first, axis=0).astype(jnp.float32)
        right = jnp.take(day_spec, second, axis=0).astype(jnp.float32)
        left_re, left_im = (left[:, :F], left[:, F:])
        right_re, right_im = (right[:, :F], right[:, F:])
        cross_re = left_re * right_re + left_im * right_im
        cross_im = left_im * right_re - left_re * right_im
        cross = jnp.concatenate([cross_re, cross_im], 1).astype(jnp.bfloat16)
        analytic = lax.dot_general(table, cross, (((1,), (1,)), ((), ())), preferred_element_type=jnp.float32)
        trace = analytic[:LAGS]
        hilbert = analytic[LAGS:]
        amplitude = jnp.sqrt(trace * trace + hilbert * hilbert)
        inverse = 1.0 / jnp.maximum(amplitude, 0.5)
        lin_sum, real_sum, imag_sum = carry
        lin_sum = lin_sum + weight[None, :] * trace
        real_sum = real_sum + weight[None, :] * (trace * inverse)
        imag_sum = imag_sum + weight[None, :] * (hilbert * inverse)
        return ((lin_sum, real_sum, imag_sum), None)
    zeros = jnp.zeros((LAGS, pair_list.shape[0]), jnp.float32)
    (lin_sum, real_sum, imag_sum), _ = lax.scan(one_day, (zeros, zeros, zeros), (spectra, weights))
    count = lax.optimization_barrier(jnp.sum(weights, 0))[None, :]
    linear_stack = lin_sum / count
    weighted_stack = linear_stack * (real_sum * real_sum + imag_sum * imag_sum) / (count * count)
    return (linear_stack, weighted_stack)
```

```python
import math

import jax
import jax.numpy as jnp
from jax import lax
from jax.sharding import PartitionSpec as P

F = 512
MAXLAG = 200
LAGS = 401


def lag_table():
    lag = jnp.arange(LAGS, dtype=jnp.int32) - MAXLAG
    freq = jnp.arange(F, dtype=jnp.int32)
    phase = jnp.mod(lag[:, None] * freq[None, :], 2 * F).astype(jnp.float32) * (math.pi / F)
    scale = 1.0 / math.sqrt(F)
    cosine = jnp.cos(phase) * scale
    sine = jnp.sin(phase) * scale
    upper = jnp.concatenate([cosine, -sine], 1)
    lower = jnp.concatenate([sine, cosine], 1)
    return jnp.concatenate([upper, lower], 0).astype(jnp.bfloat16)


def per_device(spectra, pair_list, mask):
    gathered = lax.all_gather(spectra, "pair", axis=1, tiled=True)
    station_count = gathered.shape[1]
    pair_rows = pair_list.shape[0]
    first = pair_list[:, 0]
    second = pair_list[:, 1]
    column = lax.broadcasted_iota(jnp.int32, (pair_rows, station_count), 1)
    pick_first = (first[:, None] == column).astype(jnp.float32)
    pick_second = (second[:, None] == column).astype(jnp.float32)
    mask_float = mask.astype(jnp.float32)
    weights = jnp.einsum("ds,ps->dp", mask_float, pick_first) * jnp.einsum(
        "ds,ps->dp", mask_float, pick_second
    )
    count_local = jnp.sum(weights, 0)[:, None]
    table = lag_table()

    def one_day(carry, inputs):
        day_spec, weight = inputs
        left = jnp.take(day_spec, first, axis=0).astype(jnp.float32)
        right = jnp.take(day_spec, second, axis=0).astype(jnp.float32)
        half = left.shape[1] // 2
        left_re, left_im = (left[:, :half], left[:, half:])
        right_re, right_im = (right[:, :half], right[:, half:])
        cross_re = left_re * right_re + left_im * right_im
        cross_im = left_im * right_re - left_re * right_im
        cross = jnp.concatenate([cross_re, cross_im], 1).astype(jnp.bfloat16)
        analytic = lax.dot_general(
            cross, table, (((1,), (1,)), ((), ())), preferred_element_type=jnp.float32
        )
        trace = analytic[:, :LAGS]
        hilbert = analytic[:, LAGS:]
        amplitude = jnp.sqrt(trace * trace + hilbert * hilbert)
        inverse = 1.0 / jnp.maximum(amplitude, 0.5)
        w = weight[:, None]
        lin_sum, real_sum, imag_sum = carry
        lin_sum = lin_sum + w * trace
        real_sum = real_sum + w * (trace * inverse)
        imag_sum = imag_sum + w * (hilbert * inverse)
        return ((lin_sum, real_sum, imag_sum), None)

    zeros = jnp.zeros((pair_rows, LAGS), jnp.float32)
    (lin_sum, real_sum, imag_sum), _ = lax.scan(one_day, (zeros, zeros, zeros), (gathered, weights))
    packed = jnp.concatenate([lin_sum, real_sum, imag_sum, count_local], 1)
    own = lax.psum_scatter(packed, "day", scatter_dimension=0, tiled=True)
    lin_own = own[:, :LAGS]
    real_own = own[:, LAGS : 2 * LAGS]
    imag_own = own[:, 2 * LAGS : 3 * LAGS]
    count_own = own[:, 3 * LAGS :]
    linear_stack = lin_own / count_own
    weighted_stack = (
        linear_stack * (real_own * real_own + imag_own * imag_own) / (count_own * count_own)
    )
    return (linear_stack.T, weighted_stack.T)


def solution(mesh):
    in_specs = (P("day", "pair", None), P("pair", None), P("day", None))
    out_specs = (P(None, ("pair", "day")), P(None, ("pair", "day")))
    return jax.shard_map(
        per_device, mesh=mesh, in_specs=in_specs, out_specs=out_specs, check_vma=False
    )
```

```python
import math

import jax
import jax.numpy as jnp
from jax import lax
from jax.sharding import PartitionSpec as P

F = 512
MAXLAG = 200
LAGS = 401


def lag_table():
    lag = jnp.arange(LAGS, dtype=jnp.int32) - MAXLAG
    freq = jnp.arange(F, dtype=jnp.int32)
    phase = jnp.mod(lag[:, None] * freq[None, :], 2 * F).astype(jnp.float32) * (math.pi / F)
    scale = 1.0 / math.sqrt(F)
    cosine = jnp.cos(phase) * scale
    sine = jnp.sin(phase) * scale
    upper = jnp.concatenate([cosine, -sine], 1)
    lower = jnp.concatenate([sine, cosine], 1)
    return jnp.concatenate([upper, lower], 0).astype(jnp.bfloat16)


def per_device(spectra, pair_list, mask):
    g = lax.all_gather(spectra, "zh", axis=1, tiled=True)
    gathered = lax.all_gather(g, "y", axis=1, tiled=True)
    station_count = gathered.shape[1]
    pair_rows = pair_list.shape[0]
    first = pair_list[:, 0]
    second = pair_list[:, 1]
    column = lax.broadcasted_iota(jnp.int32, (pair_rows, station_count), 1)
    pick_first = (first[:, None] == column).astype(jnp.float32)
    pick_second = (second[:, None] == column).astype(jnp.float32)
    mask_float = mask.astype(jnp.float32)
    weights = jnp.einsum("ds,ps->dp", mask_float, pick_first) * jnp.einsum(
        "ds,ps->dp", mask_float, pick_second
    )
    count_local = jnp.sum(weights, 0)[:, None]
    table = lag_table()

    def one_day(carry, inputs):
        day_spec, weight = inputs
        left = jnp.take(day_spec, first, axis=0).astype(jnp.float32)
        right = jnp.take(day_spec, second, axis=0).astype(jnp.float32)
        half = left.shape[1] // 2
        left_re, left_im = (left[:, :half], left[:, half:])
        right_re, right_im = (right[:, :half], right[:, half:])
        cross_re = left_re * right_re + left_im * right_im
        cross_im = left_im * right_re - left_re * right_im
        cross = jnp.concatenate([cross_re, cross_im], 1).astype(jnp.bfloat16)
        analytic = lax.dot_general(
            cross, table, (((1,), (1,)), ((), ())), preferred_element_type=jnp.float32
        )
        trace = analytic[:, :LAGS]
        hilbert = analytic[:, LAGS:]
        amplitude = jnp.sqrt(trace * trace + hilbert * hilbert)
        inverse = 1.0 / jnp.maximum(amplitude, 0.5)
        w = weight[:, None]
        lin_sum, real_sum, imag_sum = carry
        lin_sum = lin_sum + w * trace
        real_sum = real_sum + w * (trace * inverse)
        imag_sum = imag_sum + w * (hilbert * inverse)
        return ((lin_sum, real_sum, imag_sum), None)

    zeros = jnp.zeros((pair_rows, LAGS), jnp.float32)
    (lin_sum, real_sum, imag_sum), _ = lax.scan(one_day, (zeros, zeros, zeros), (gathered, weights))
    packed = jnp.concatenate([lin_sum, real_sum, imag_sum, count_local], 1)
    cols = packed.shape[1]
    p = packed.reshape(4, 8, 2, 8, cols).transpose(2, 1, 0, 3, 4).reshape(512, cols)
    p = lax.psum_scatter(p, "c", scatter_dimension=0, tiled=True)
    p = lax.psum_scatter(p, "zl", scatter_dimension=0, tiled=True)
    own = lax.psum_scatter(p, "x", scatter_dimension=0, tiled=True)
    lin_own = own[:, :LAGS]
    real_own = own[:, LAGS : 2 * LAGS]
    imag_own = own[:, 2 * LAGS : 3 * LAGS]
    count_own = own[:, 3 * LAGS :]
    linear_stack = lin_own / count_own
    weighted_stack = (
        linear_stack * (real_own * real_own + imag_own * imag_own) / (count_own * count_own)
    )
    return (linear_stack.T, weighted_stack.T)


def solution(mesh):
    from jax.sharding import Mesh
    devs = mesh.devices.reshape(4, 8, 2, 4, 2)
    m = Mesh(devs, ("x", "zl", "c", "y", "zh"))
    day = ("x", "zl", "c")
    pair = ("y", "zh")
    in_specs = (P(day, pair, None), P(pair, None), P(day, None))
    out_specs = (P(None, pair + day), P(None, pair + day))
    return jax.shard_map(per_device, mesh=m, in_specs=in_specs, out_specs=out_specs, check_vma=False)
```

```python
import math

import jax
import jax.numpy as jnp
from jax import lax
from jax.sharding import PartitionSpec as P

F = 512
MAXLAG = 200
LAGS = 401


def lag_table():
    lag = jnp.arange(LAGS, dtype=jnp.int32) - MAXLAG
    freq = jnp.arange(F, dtype=jnp.int32)
    phase = jnp.mod(lag[:, None] * freq[None, :], 2 * F).astype(jnp.float32) * (math.pi / F)
    scale = 1.0 / math.sqrt(F)
    cosine = jnp.cos(phase) * scale
    sine = jnp.sin(phase) * scale
    upper = jnp.concatenate([cosine, -sine], 1)
    lower = jnp.concatenate([sine, cosine], 1)
    return jnp.concatenate([upper, lower], 0).astype(jnp.bfloat16)


def per_device(spectra, pair_list, mask):
    g = lax.all_gather(spectra, "zh", axis=1, tiled=True)
    g = lax.all_gather(g, "y", axis=1, tiled=True)
    gathered = lax.all_gather(g, "c", axis=0, tiled=True)
    mask = lax.all_gather(mask, "c", axis=0, tiled=True)
    core = lax.axis_index("c")
    nx, nz, nc = 4, 8, 2
    k = pair_list.shape[0] // (nx * nz * nc)
    pl = pair_list.reshape(nx, nz, nc, k, 2)
    pl = lax.dynamic_index_in_dim(pl, core, 2, keepdims=False)
    pl = pl.transpose(1, 0, 2, 3).reshape(nz * nx * k, 2)
    station_count = gathered.shape[1]
    pair_rows = pl.shape[0]
    first = pl[:, 0]
    second = pl[:, 1]
    column = lax.broadcasted_iota(jnp.int32, (pair_rows, station_count), 1)
    pick_first = (first[:, None] == column).astype(jnp.float32)
    pick_second = (second[:, None] == column).astype(jnp.float32)
    mask_float = mask.astype(jnp.float32)
    weights = jnp.einsum("ds,ps->dp", mask_float, pick_first) * jnp.einsum(
        "ds,ps->dp", mask_float, pick_second
    )
    count_local = jnp.sum(weights, 0)[:, None]
    table = lag_table()

    def one_day(carry, inputs):
        day_spec, weight = inputs
        left = jnp.take(day_spec, first, axis=0).astype(jnp.float32)
        right = jnp.take(day_spec, second, axis=0).astype(jnp.float32)
        half = left.shape[1] // 2
        left_re, left_im = (left[:, :half], left[:, half:])
        right_re, right_im = (right[:, :half], right[:, half:])
        cross_re = left_re * right_re + left_im * right_im
        cross_im = left_im * right_re - left_re * right_im
        cross = jnp.concatenate([cross_re, cross_im], 1).astype(jnp.bfloat16)
        analytic = lax.dot_general(
            cross, table, (((1,), (1,)), ((), ())), preferred_element_type=jnp.float32
        )
        trace = analytic[:, :LAGS]
        hilbert = analytic[:, LAGS:]
        amplitude = jnp.sqrt(trace * trace + hilbert * hilbert)
        inverse = 1.0 / jnp.maximum(amplitude, 0.5)
        w = weight[:, None]
        lin_sum, real_sum, imag_sum = carry
        lin_sum = lin_sum + w * trace
        real_sum = real_sum + w * (trace * inverse)
        imag_sum = imag_sum + w * (hilbert * inverse)
        return ((lin_sum, real_sum, imag_sum), None)

    zeros = jnp.zeros((pair_rows, LAGS), jnp.float32)
    (lin_sum, real_sum, imag_sum), _ = lax.scan(one_day, (zeros, zeros, zeros), (gathered, weights))
    packed = jnp.concatenate([lin_sum, real_sum, imag_sum, count_local], 1)
    cols = packed.shape[1]
    own = lax.all_to_all(packed.reshape(32, -1, cols), ("zl", "x"), 0, 0, tiled=True).sum(0)
    lin_own = own[:, :LAGS]
    real_own = own[:, LAGS : 2 * LAGS]
    imag_own = own[:, 2 * LAGS : 3 * LAGS]
    count_own = own[:, 3 * LAGS :]
    linear_stack = lin_own / count_own
    weighted_stack = (
        linear_stack * (real_own * real_own + imag_own * imag_own) / (count_own * count_own)
    )
    return (linear_stack.T, weighted_stack.T)


def solution(mesh):
    from jax.sharding import Mesh
    devs = mesh.devices.reshape(4, 8, 2, 4, 2)
    m = Mesh(devs, ("x", "zl", "c", "y", "zh"))
    day = ("x", "zl", "c")
    pair = ("y", "zh")
    in_specs = (P(day, pair, None), P(pair, None), P(day, None))
    out_specs = (P(None, pair + day), P(None, pair + day))
    return jax.shard_map(per_device, mesh=m, in_specs=in_specs, out_specs=out_specs, check_vma=False)
```

```python
import math

import jax
import jax.numpy as jnp
from jax import lax
from jax.sharding import PartitionSpec as P

F = 512
MAXLAG = 200
LAGS = 401


def lag_table():
    lag = jnp.arange(LAGS, dtype=jnp.int32) - MAXLAG
    freq = jnp.arange(F, dtype=jnp.int32)
    phase = jnp.mod(lag[:, None] * freq[None, :], 2 * F).astype(jnp.float32) * (math.pi / F)
    scale = 1.0 / math.sqrt(F)
    cosine = jnp.cos(phase) * scale
    sine = jnp.sin(phase) * scale
    upper = jnp.concatenate([cosine, -sine], 1)
    lower = jnp.concatenate([sine, cosine], 1)
    return jnp.concatenate([upper, lower], 0).astype(jnp.bfloat16)


def day_sums(days, mask_days, first, second, table):
    station_count = days.shape[1]
    pair_rows = first.shape[0]
    column = lax.broadcasted_iota(jnp.int32, (pair_rows, station_count), 1)
    pick_first = (first[:, None] == column).astype(jnp.float32)
    pick_second = (second[:, None] == column).astype(jnp.float32)
    mask_float = mask_days.astype(jnp.float32)
    weights = jnp.einsum("ds,ps->dp", mask_float, pick_first) * jnp.einsum(
        "ds,ps->dp", mask_float, pick_second
    )
    count = jnp.sum(weights, 0)[:, None]
    left = jnp.take(days, first, axis=1).astype(jnp.float32)
    right = jnp.take(days, second, axis=1).astype(jnp.float32)
    half = left.shape[2] // 2
    left_re, left_im = (left[..., :half], left[..., half:])
    right_re, right_im = (right[..., :half], right[..., half:])
    cross_re = left_re * right_re + left_im * right_im
    cross_im = left_im * right_re - left_re * right_im
    cross = jnp.concatenate([cross_re, cross_im], 2).astype(jnp.bfloat16)
    analytic = lax.dot_general(
        cross, table, (((2,), (1,)), ((), ())), preferred_element_type=jnp.float32
    )
    trace = analytic[..., :LAGS]
    hilbert = analytic[..., LAGS:]
    amplitude = jnp.sqrt(trace * trace + hilbert * hilbert)
    inverse = 1.0 / jnp.maximum(amplitude, 0.5)
    w = weights[:, :, None]
    lin_sum = jnp.sum(w * trace, 0)
    real_sum = jnp.sum(w * (trace * inverse), 0)
    imag_sum = jnp.sum(w * (hilbert * inverse), 0)
    return lin_sum, real_sum, imag_sum, count


def per_device(spectra, pair_list, mask):
    g = lax.all_gather(spectra, "zh", axis=1, tiled=True)
    g = lax.all_gather(g, "y", axis=1, tiled=True)
    core = lax.axis_index("c")
    swap = [(0, 1), (1, 0)]
    g_other = lax.ppermute(g, "c", swap)
    mask_other = lax.ppermute(mask, "c", swap)
    nx, nz, nc = 4, 8, 2
    k = pair_list.shape[0] // (nx * nz * nc)
    pl = pair_list.reshape(nx, nz, nc, k, 2)
    pl = lax.dynamic_index_in_dim(pl, core, 2, keepdims=False)
    pl = pl.transpose(1, 0, 2, 3).reshape(nz * nx * k, 2)
    first = pl[:, 0]
    second = pl[:, 1]
    table = lag_table()
    mine = day_sums(g, mask, first, second, table)
    theirs = day_sums(g_other, mask_other, first, second, table)
    sums = [a + b for a, b in zip(mine, theirs)]
    packed = jnp.concatenate(list(sums), 1)
    cols = packed.shape[1]
    own = lax.all_to_all(packed.reshape(32, -1, cols), ("zl", "x"), 0, 0, tiled=True).sum(0)
    lin_own = own[:, :LAGS]
    real_own = own[:, LAGS : 2 * LAGS]
    imag_own = own[:, 2 * LAGS : 3 * LAGS]
    count_own = own[:, 3 * LAGS :]
    linear_stack = lin_own / count_own
    weighted_stack = (
        linear_stack * (real_own * real_own + imag_own * imag_own) / (count_own * count_own)
    )
    return (linear_stack.T, weighted_stack.T)


def solution(mesh):
    from jax.sharding import Mesh
    devs = mesh.devices.reshape(4, 8, 2, 4, 2)
    m = Mesh(devs, ("x", "zl", "c", "y", "zh"))
    day = ("x", "zl", "c")
    pair = ("y", "zh")
    in_specs = (P(day, pair, None), P(pair, None), P(day, None))
    out_specs = (P(None, pair + day), P(None, pair + day))
    return jax.shard_map(per_device, mesh=m, in_specs=in_specs, out_specs=out_specs, check_vma=False)
```

```python
import math

import jax
import jax.numpy as jnp
from jax import lax
from jax.sharding import PartitionSpec as P

F = 512
MAXLAG = 200
LAGS = 401


def lag_table():
    lag = jnp.arange(LAGS, dtype=jnp.int32) - MAXLAG
    freq = jnp.arange(F, dtype=jnp.int32)
    phase = jnp.mod(lag[:, None] * freq[None, :], 2 * F).astype(jnp.float32) * (math.pi / F)
    scale = 1.0 / math.sqrt(F)
    cosine = jnp.cos(phase) * scale
    sine = jnp.sin(phase) * scale
    upper = jnp.concatenate([cosine, -sine], 1)
    lower = jnp.concatenate([sine, cosine], 1)
    return jnp.concatenate([upper, lower], 0).astype(jnp.bfloat16)


def day_sums(days, mask_days, first, second, table):
    station_count = days.shape[1]
    pair_rows = first.shape[0]
    column = lax.broadcasted_iota(jnp.int32, (pair_rows, station_count), 1)
    pick_first = (first[:, None] == column).astype(jnp.float32)
    pick_second = (second[:, None] == column).astype(jnp.float32)
    mask_float = mask_days.astype(jnp.float32)
    weights = jnp.einsum("ds,ps->dp", mask_float, pick_first) * jnp.einsum(
        "ds,ps->dp", mask_float, pick_second
    )
    count = jnp.sum(weights, 0)[:, None]
    left = jnp.take(days, first, axis=1).astype(jnp.float32)
    right = jnp.take(days, second, axis=1).astype(jnp.float32)
    half = left.shape[2] // 2
    left_re, left_im = (left[..., :half], left[..., half:])
    right_re, right_im = (right[..., :half], right[..., half:])
    cross_re = left_re * right_re + left_im * right_im
    cross_im = left_im * right_re - left_re * right_im
    cross = jnp.concatenate([cross_re, cross_im], 2).astype(jnp.bfloat16)
    analytic = lax.dot_general(
        cross, table, (((2,), (1,)), ((), ())), preferred_element_type=jnp.float32
    )
    trace = analytic[..., :LAGS]
    hilbert = analytic[..., LAGS:]
    amplitude = jnp.sqrt(trace * trace + hilbert * hilbert)
    inverse = 1.0 / jnp.maximum(amplitude, 0.5)
    w = weights[:, :, None]
    lin_sum = jnp.sum(w * trace, 0)
    real_sum = jnp.sum(w * (trace * inverse), 0)
    imag_sum = jnp.sum(w * (hilbert * inverse), 0)
    return lin_sum, real_sum, imag_sum, count


def per_device(spectra, pair_list, mask):
    g = lax.all_gather(spectra, "zh", axis=1, tiled=True)
    g = lax.all_gather(g, "y", axis=1, tiled=True)
    core = lax.axis_index("c")
    swap = [(0, 1), (1, 0)]
    g_other = lax.ppermute(g, "c", swap)
    mask_other = lax.ppermute(mask, "c", swap)
    nx, nz, nc = 4, 8, 2
    k = pair_list.shape[0] // (nx * nz * nc)
    pl = pair_list.reshape(nx, nz, nc, k, 2)
    pl = lax.dynamic_index_in_dim(pl, core, 2, keepdims=False)
    pl = pl.transpose(1, 0, 2, 3).reshape(nz * nx * k, 2)
    first = pl[:, 0]
    second = pl[:, 1]
    table = lag_table()
    mine = day_sums(g, mask, first, second, table)
    theirs = day_sums(g_other, mask_other, first, second, table)
    sums = [a + b for a, b in zip(mine, theirs)]
    packed = jnp.concatenate(list(sums), 1)
    cols = packed.shape[1]
    p = lax.all_to_all(packed.reshape(8, 4, -1, cols).transpose(1, 0, 2, 3), "x", 0, 0, tiled=True).sum(0)
    own = lax.all_to_all(p, "zl", 0, 0, tiled=True).sum(0)
    lin_own = own[:, :LAGS]
    real_own = own[:, LAGS : 2 * LAGS]
    imag_own = own[:, 2 * LAGS : 3 * LAGS]
    count_own = own[:, 3 * LAGS :]
    linear_stack = lin_own / count_own
    weighted_stack = (
        linear_stack * (real_own * real_own + imag_own * imag_own) / (count_own * count_own)
    )
    return (linear_stack.T, weighted_stack.T)


def solution(mesh):
    from jax.sharding import Mesh
    devs = mesh.devices.reshape(4, 8, 2, 4, 2)
    m = Mesh(devs, ("x", "zl", "c", "y", "zh"))
    day = ("x", "zl", "c")
    pair = ("y", "zh")
    in_specs = (P(day, pair, None), P(pair, None), P(day, None))
    out_specs = (P(None, pair + day), P(None, pair + day))
    return jax.shard_map(per_device, mesh=m, in_specs=in_specs, out_specs=out_specs, check_vma=False)
```

```python
import math

import jax
import jax.numpy as jnp
from jax import lax
from jax.sharding import PartitionSpec as P

F = 512
MAXLAG = 200
LAGS = 401


def lag_table():
    lag = jnp.arange(LAGS, dtype=jnp.int32) - MAXLAG
    freq = jnp.arange(F, dtype=jnp.int32)
    phase = jnp.mod(lag[:, None] * freq[None, :], 2 * F).astype(jnp.float32) * (math.pi / F)
    scale = 1.0 / math.sqrt(F)
    cosine = jnp.cos(phase) * scale
    sine = jnp.sin(phase) * scale
    upper = jnp.concatenate([cosine, -sine], 1)
    lower = jnp.concatenate([sine, cosine], 1)
    return jnp.concatenate([upper, lower], 0).astype(jnp.bfloat16)


def day_sums(days, mask_days, first, second, table):
    station_count = days.shape[1]
    pair_rows = first.shape[0]
    column = lax.broadcasted_iota(jnp.int32, (pair_rows, station_count), 1)
    pick_first = (first[:, None] == column).astype(jnp.float32)
    pick_second = (second[:, None] == column).astype(jnp.float32)
    mask_float = mask_days.astype(jnp.float32)
    weights = jnp.einsum("ds,ps->dp", mask_float, pick_first) * jnp.einsum(
        "ds,ps->dp", mask_float, pick_second
    )
    count = jnp.sum(weights, 0)[:, None]
    left = jnp.einsum(
        "ps,dsf->dpf", pick_first.astype(days.dtype), days, preferred_element_type=jnp.float32
    )
    right = jnp.einsum(
        "ps,dsf->dpf", pick_second.astype(days.dtype), days, preferred_element_type=jnp.float32
    )
    half = left.shape[2] // 2
    left_re, left_im = (left[..., :half], left[..., half:])
    right_re, right_im = (right[..., :half], right[..., half:])
    cross_re = left_re * right_re + left_im * right_im
    cross_im = left_im * right_re - left_re * right_im
    cross = jnp.concatenate([cross_re, cross_im], 2).astype(jnp.bfloat16)
    analytic = lax.dot_general(
        cross, table, (((2,), (1,)), ((), ())), preferred_element_type=jnp.float32
    )
    trace = analytic[..., :LAGS]
    hilbert = analytic[..., LAGS:]
    amplitude = jnp.sqrt(trace * trace + hilbert * hilbert)
    inverse = 1.0 / jnp.maximum(amplitude, 0.5)
    w = weights[:, :, None]
    lin_sum = jnp.sum(w * trace, 0)
    real_sum = jnp.sum(w * (trace * inverse), 0)
    imag_sum = jnp.sum(w * (hilbert * inverse), 0)
    return lin_sum, real_sum, imag_sum, count


def per_device(spectra, pair_list, mask):
    g = lax.all_gather(spectra, "zh", axis=1, tiled=True)
    g = lax.all_gather(g, "y", axis=1, tiled=True)
    core = lax.axis_index("c")
    swap = [(0, 1), (1, 0)]
    g_other = lax.ppermute(g, "c", swap)
    mask_other = lax.ppermute(mask, "c", swap)
    nx, nz, nc = 4, 8, 2
    k = pair_list.shape[0] // (nx * nz * nc)
    pl = pair_list.reshape(nx, nz, nc, k, 2)
    pl = lax.dynamic_index_in_dim(pl, core, 2, keepdims=False)
    pl = pl.transpose(1, 0, 2, 3).reshape(nz * nx * k, 2)
    first = pl[:, 0]
    second = pl[:, 1]
    table = lag_table()
    mine = day_sums(g, mask, first, second, table)
    theirs = day_sums(g_other, mask_other, first, second, table)
    sums = [a + b for a, b in zip(mine, theirs)]
    packed = jnp.concatenate(list(sums), 1)
    cols = packed.shape[1]
    p = lax.all_to_all(packed.reshape(8, 4, -1, cols).transpose(1, 0, 2, 3), "x", 0, 0, tiled=True).sum(0)
    own = lax.all_to_all(p, "zl", 0, 0, tiled=True).sum(0)
    lin_own = own[:, :LAGS]
    real_own = own[:, LAGS : 2 * LAGS]
    imag_own = own[:, 2 * LAGS : 3 * LAGS]
    count_own = own[:, 3 * LAGS :]
    linear_stack = lin_own / count_own
    weighted_stack = (
        linear_stack * (real_own * real_own + imag_own * imag_own) / (count_own * count_own)
    )
    return (linear_stack.T, weighted_stack.T)


def solution(mesh):
    from jax.sharding import Mesh
    devs = mesh.devices.reshape(4, 8, 2, 4, 2)
    m = Mesh(devs, ("x", "zl", "c", "y", "zh"))
    day = ("x", "zl", "c")
    pair = ("y", "zh")
    in_specs = (P(day, pair, None), P(pair, None), P(day, None))
    out_specs = (P(None, pair + day), P(None, pair + day))
    return jax.shard_map(per_device, mesh=m, in_specs=in_specs, out_specs=out_specs, check_vma=False)
```

```python
import math

import jax
import jax.numpy as jnp
from jax import lax
from jax.sharding import PartitionSpec as P

F = 512
MAXLAG = 200
LAGS = 401


def lag_table():
    lag = jnp.arange(LAGS, dtype=jnp.int32) - MAXLAG
    freq = jnp.arange(F, dtype=jnp.int32)
    phase = jnp.mod(lag[:, None] * freq[None, :], 2 * F).astype(jnp.float32) * (math.pi / F)
    scale = 1.0 / math.sqrt(F)
    cosine = jnp.cos(phase) * scale
    sine = jnp.sin(phase) * scale
    upper = jnp.concatenate([cosine, -sine], 1)
    lower = jnp.concatenate([sine, cosine], 1)
    return jnp.concatenate([upper, lower], 0).astype(jnp.bfloat16)


def day_sums(days, mask_days, first, second, table):
    station_count = days.shape[1]
    pair_rows = first.shape[0]
    column = lax.broadcasted_iota(jnp.int32, (pair_rows, station_count), 1)
    pick_first = (first[:, None] == column).astype(jnp.float32)
    pick_second = (second[:, None] == column).astype(jnp.float32)
    mask_float = mask_days.astype(jnp.float32)
    weights = jnp.einsum("ds,ps->dp", mask_float, pick_first) * jnp.einsum(
        "ds,ps->dp", mask_float, pick_second
    )
    count = jnp.sum(weights, 0)[:, None]
    left = jnp.einsum(
        "ps,dsf->dpf", pick_first.astype(days.dtype), days, preferred_element_type=jnp.float32
    )
    right = jnp.einsum(
        "ps,dsf->dpf", pick_second.astype(days.dtype), days, preferred_element_type=jnp.float32
    )
    half = left.shape[2] // 2
    left_re, left_im = (left[..., :half], left[..., half:])
    right_re, right_im = (right[..., :half], right[..., half:])
    cross_re = left_re * right_re + left_im * right_im
    cross_im = left_im * right_re - left_re * right_im
    cross = jnp.concatenate([cross_re, cross_im], 2).astype(jnp.bfloat16)
    analytic = lax.dot_general(
        cross, table, (((2,), (1,)), ((), ())), preferred_element_type=jnp.float32
    )
    trace = analytic[..., :LAGS]
    hilbert = analytic[..., LAGS:]
    amplitude = jnp.sqrt(trace * trace + hilbert * hilbert)
    inverse = 1.0 / jnp.maximum(amplitude, 0.5)
    w = weights[:, :, None]
    lin_sum = jnp.sum(w * trace, 0)
    real_sum = jnp.sum(w * (trace * inverse), 0)
    imag_sum = jnp.sum(w * (hilbert * inverse), 0)
    return lin_sum, real_sum, imag_sum, count


def per_device(spectra, pair_list, mask):
    g = lax.all_gather(spectra, "zh", axis=1, tiled=True)
    rep = jnp.broadcast_to(g[None], (4,) + g.shape)
    got = lax.all_to_all(rep, "y", 0, 0, tiled=True)
    g = got.transpose(1, 0, 2, 3).reshape(g.shape[0], 4 * g.shape[1], g.shape[2])
    core = lax.axis_index("c")
    swap = [(0, 1), (1, 0)]
    g_other = lax.ppermute(g, "c", swap)
    mask_other = lax.ppermute(mask, "c", swap)
    nx, nz, nc = 4, 8, 2
    k = pair_list.shape[0] // (nx * nz * nc)
    pl = pair_list.reshape(nx, nz, nc, k, 2)
    pl = lax.dynamic_index_in_dim(pl, core, 2, keepdims=False)
    pl = pl.transpose(1, 0, 2, 3).reshape(nz * nx * k, 2)
    first = pl[:, 0]
    second = pl[:, 1]
    table = lag_table()
    mine = day_sums(g, mask, first, second, table)
    theirs = day_sums(g_other, mask_other, first, second, table)
    sums = [a + b for a, b in zip(mine, theirs)]
    packed = jnp.concatenate(list(sums), 1)
    cols = packed.shape[1]
    p = lax.all_to_all(packed.reshape(8, 4, -1, cols).transpose(1, 0, 2, 3), "x", 0, 0, tiled=True).sum(0)
    own = lax.all_to_all(p, "zl", 0, 0, tiled=True).sum(0)
    lin_own = own[:, :LAGS]
    real_own = own[:, LAGS : 2 * LAGS]
    imag_own = own[:, 2 * LAGS : 3 * LAGS]
    count_own = own[:, 3 * LAGS :]
    linear_stack = lin_own / count_own
    weighted_stack = (
        linear_stack * (real_own * real_own + imag_own * imag_own) / (count_own * count_own)
    )
    return (linear_stack.T, weighted_stack.T)


def solution(mesh):
    from jax.sharding import Mesh
    devs = mesh.devices.reshape(4, 8, 2, 4, 2)
    m = Mesh(devs, ("x", "zl", "c", "y", "zh"))
    day = ("x", "zl", "c")
    pair = ("y", "zh")
    in_specs = (P(day, pair, None), P(pair, None), P(day, None))
    out_specs = (P(None, pair + day), P(None, pair + day))
    return jax.shard_map(per_device, mesh=m, in_specs=in_specs, out_specs=out_specs, check_vma=False)
```

```python
import math

import jax
import jax.numpy as jnp
from jax import lax
from jax.sharding import PartitionSpec as P

F = 512
MAXLAG = 200
LAGS = 401


def lag_table():
    lag = jnp.arange(LAGS, dtype=jnp.int32) - MAXLAG
    freq = jnp.arange(F, dtype=jnp.int32)
    phase = jnp.mod(lag[:, None] * freq[None, :], 2 * F).astype(jnp.float32) * (math.pi / F)
    scale = 1.0 / math.sqrt(F)
    cosine = jnp.cos(phase) * scale
    sine = jnp.sin(phase) * scale
    upper = jnp.concatenate([cosine, -sine], 1)
    lower = jnp.concatenate([sine, cosine], 1)
    return jnp.concatenate([upper, lower], 0).astype(jnp.bfloat16)


def day_sums(days, mask_days, first, second, table):
    station_count = days.shape[1]
    pair_rows = first.shape[0]
    column = lax.broadcasted_iota(jnp.int32, (pair_rows, station_count), 1)
    pick_first = (first[:, None] == column).astype(jnp.float32)
    pick_second = (second[:, None] == column).astype(jnp.float32)
    mask_float = mask_days.astype(jnp.float32)
    weights = jnp.einsum("ds,ps->dp", mask_float, pick_first) * jnp.einsum(
        "ds,ps->dp", mask_float, pick_second
    )
    count = jnp.sum(weights, 0)[:, None]
    left = jnp.einsum(
        "ps,dsf->dpf", pick_first.astype(days.dtype), days, preferred_element_type=jnp.float32
    )
    right = jnp.einsum(
        "ps,dsf->dpf", pick_second.astype(days.dtype), days, preferred_element_type=jnp.float32
    )
    half = left.shape[2] // 2
    left_re, left_im = (left[..., :half], left[..., half:])
    right_re, right_im = (right[..., :half], right[..., half:])
    cross_re = left_re * right_re + left_im * right_im
    cross_im = left_im * right_re - left_re * right_im
    cross = jnp.concatenate([cross_re, cross_im], 2).astype(jnp.bfloat16)
    analytic = lax.dot_general(
        cross, table, (((2,), (1,)), ((), ())), preferred_element_type=jnp.float32
    )
    trace = analytic[..., :LAGS]
    hilbert = analytic[..., LAGS:]
    amplitude = jnp.sqrt(trace * trace + hilbert * hilbert)
    inverse = 1.0 / jnp.maximum(amplitude, 0.5)
    w = weights[:, :, None]
    lin_sum = jnp.sum(w * trace, 0)
    real_sum = jnp.sum(w * (trace * inverse), 0)
    imag_sum = jnp.sum(w * (hilbert * inverse), 0)
    return lin_sum, real_sum, imag_sum, count


def per_device(spectra, pair_list, mask):
    g = lax.all_gather(spectra, "zh", axis=1, tiled=True)
    rep = jnp.broadcast_to(g[None], (4,) + g.shape)
    got = lax.all_to_all(rep, "y", 0, 0, tiled=True)
    g = got.transpose(1, 0, 2, 3).reshape(g.shape[0], 4 * g.shape[1], g.shape[2])
    core = lax.axis_index("c")
    swap = [(0, 1), (1, 0)]
    g_other = lax.ppermute(g, "c", swap)
    mask_other = lax.ppermute(mask, "c", swap)
    nx, nz, nc = 4, 8, 2
    k = pair_list.shape[0] // (nx * nz * nc)
    pl = pair_list.reshape(nx, nz, nc, k, 2)
    pl = lax.dynamic_index_in_dim(pl, core, 2, keepdims=False)
    pl = pl.reshape(nx * nz * k, 2)
    first = pl[:, 0]
    second = pl[:, 1]
    table = lag_table()
    mine = day_sums(g, mask, first, second, table)
    theirs = day_sums(g_other, mask_other, first, second, table)
    sums = [a + b for a, b in zip(mine, theirs)]
    width = sum(x.shape[1] for x in sums)
    pad = jnp.zeros((sums[0].shape[0], -width % 128), jnp.float32)
    packed = jnp.concatenate(list(sums) + [pad], 1)
    cols = packed.shape[1]
    p = lax.all_to_all(packed.reshape(4, 8, -1, cols), "x", 0, 0, tiled=True).sum(0)
    own = lax.all_to_all(p, "zl", 0, 0, tiled=True).sum(0)
    lin_own = own[:, :LAGS]
    real_own = own[:, LAGS : 2 * LAGS]
    imag_own = own[:, 2 * LAGS : 3 * LAGS]
    count_own = own[:, 3 * LAGS : 3 * LAGS + 1]
    linear_stack = lin_own / count_own
    weighted_stack = (
        linear_stack * (real_own * real_own + imag_own * imag_own) / (count_own * count_own)
    )
    return (linear_stack.T, weighted_stack.T)


def solution(mesh):
    from jax.sharding import Mesh
    devs = mesh.devices.reshape(4, 8, 2, 4, 2)
    m = Mesh(devs, ("x", "zl", "c", "y", "zh"))
    day = ("x", "zl", "c")
    pair = ("y", "zh")
    in_specs = (P(day, pair, None), P(pair, None), P(day, None))
    out_specs = (P(None, pair + day), P(None, pair + day))
    return jax.shard_map(per_device, mesh=m, in_specs=in_specs, out_specs=out_specs, check_vma=False)
```
